256 devices in a mesh: group: 16 (over y_hi, x, core), leaf: 16 (over y_lo, z).
Axes of the slice: x: 4, y: 4 (y_hi: 2, y_lo: 2; y = y_hi * 2 + y_lo), z: 8, core: 2. Of those that a mesh axis runs over, the one named last changes fastest.
Arguments:
- leaf_mass: bfloat16 [256, 512, 512], P(('group', 'leaf')), may hold values from -23 to 23, as said below
- leaf_damp: bfloat16 [256, 512, 512], P(('group', 'leaf')), may hold values from -12 to 12, as said below
- mass_coupling: bfloat16 [256, 512, 1536], P(('group', 'leaf')), may hold values from -6 to 6
- damp_coupling: bfloat16 [256, 512, 1536], P(('group', 'leaf')), may hold values from -6 to 6
- leaf_modes: bfloat16 [256, 512, 1536], P(('group', 'leaf')), may hold values from -0.15625 to 0.15625
- interface_blocks: int32 [256, 12], P(('group', 'leaf')), may hold values from 0 to 11, each once within a row
- mid_modes: bfloat16 [16, 1536, 256], P('group', 'leaf'), may hold values from -0.15625 to 0.15625
- mid_constraint: bfloat16 [16, 1536, 1024], P('group', 'leaf'), may hold values from -0.109375 to 0.109375
Outputs:
- coupling_mass: float32 [256, 512, 256], P(('group', 'leaf'))
- coupling_damp: float32 [256, 512, 256], P(('group', 'leaf'))
- modal_mass: float32 [16, 256, 1280], P('group', 'leaf')
- modal_damp: float32 [16, 256, 1280], P('group', 'leaf')
- root_mass: float32 [1024, 1024], P(('group', 'leaf'))
- root_damp: float32 [1024, 1024], P(('group', 'leaf'))
The draws below stay inside these ranges and needn't reach their ends.
Inputs may be any that keep to these rules, and one draw needn't show every extreme that they name: `interface_blocks`: each row is a permutation of 0 to 11. `leaf_mass`: each leaf's block is symmetric. `leaf_damp`: each leaf's block is symmetric.
All inputs are finite; a program needn't handle non-finite values.
Results may differ from the reference program's by a relative error of at most 0.0049.
Values may be sent and summed in bfloat16 or wider, within the bound.
No kernel may reach another device: no remote copies, remote signals or barrier semaphores. Data moves between devices by JAX's collectives and lax.ppermute only.
A program may use at most 128 MiB of HBM per device.

```python
import jax
import jax.numpy as jnp
from jax import lax

LO = 512
SEP = 1536
MODES = 256
ROOT = 1024
BLK = 128
NBLK = 12
LEAVES = 256
N_GROUP = 16
N_LEAF = 16


def symmetric_block(key, factor):
    base = jnp.clip(jax.random.normal(key, (LEAVES, LO, LO), jnp.float32), -4.0, 4.0)
    return ((base + jnp.swapaxes(base, 1, 2)) * factor).astype(jnp.bfloat16)


def draw_leaf_mass(key, part):
    return symmetric_block(jax.random.fold_in(key, 11), 2.83)


def draw_leaf_damp(key, part):
    return symmetric_block(jax.random.fold_in(key, 23), 1.4)


def with_spikes(result, stream_key, source, target, blocks, factor):
    def block_of(axis_at):
        return (jnp.arange(result.shape[axis_at]) // (result.shape[axis_at] // blocks)).reshape((-1,) + (1,) * (result.ndim - 1 - axis_at))

    one_side = jax.random.permutation(stream_key, blocks)[block_of(target)]
    other_side = (block_of(target) + blocks // 2) % blocks
    return jnp.where((block_of(source) == one_side) | (block_of(source) == other_side), factor * result, result)


def steps_of(stream_key, shape, pieces, smallest, high):
    loudness, own = 1.0, jax.random.fold_in(stream_key, 6)
    for axis_at, parts in pieces:
        steps = jnp.exp(jax.random.uniform(jax.random.fold_in(own, axis_at), (parts,), jnp.float32, smallest / len(pieces), high / len(pieces)))
        loudness = loudness * jnp.repeat(steps, shape[axis_at] // parts).reshape([-1 if axis == axis_at else 1 for axis in range(len(shape))])
    return loudness


def scatter_about(rng, dims, width, most, pieces=(), kind=jnp.bfloat16):
    values = width * jax.random.normal(rng, dims, jnp.float32)
    if pieces:
        values = values * steps_of(rng, dims, pieces, -0.22, 0.18)
    return jnp.clip(values, -most, most).astype(kind)


def gaussian_with(rng, extent, width, limit, shards, heavy, kind=jnp.bfloat16):
    array = width * jax.random.normal(rng, extent, jnp.float32)
    if shards:
        array = array * steps_of(rng, extent, shards, -0.22, 0.18)
    return jnp.clip(with_spikes(array, jax.random.fold_in(rng, 3), *heavy), -limit, limit).astype(kind)


def setup_inputs(seed: int = 0) -> dict:
    seeds = jax.random.split(jax.random.key(seed), 9)
    return {
        "leaf_mass": draw_leaf_mass(jax.random.fold_in(seeds[8], 71), 0),
        "leaf_damp": draw_leaf_damp(jax.random.fold_in(seeds[8], 71), 0),
        "mass_coupling": scatter_about(seeds[2], (LEAVES, LO, SEP), 1.0, 6.0, ((0, 256),)),
        "damp_coupling": scatter_about(seeds[3], (LEAVES, LO, SEP), 1.0, 6.0, ((0, 256),)),
        "leaf_modes": scatter_about(seeds[4], (LEAVES, LO, SEP), 0.01, 0.15625, ((0, 256),)),
        "interface_blocks": jax.vmap(lambda own: jax.random.permutation(own, NBLK))(jax.random.split(seeds[5], LEAVES)).reshape((LEAVES, NBLK)).astype(jnp.int32),
        "mid_modes": scatter_about(seeds[6], (N_GROUP, SEP, MODES), SEP ** -0.5, 0.15625, ((0, 16), (1, 16))),
        "mid_constraint": gaussian_with(seeds[7], (N_GROUP, SEP, ROOT), (SEP * 4) ** -0.5, 0.109375, ((0, 16), (1, 16)), (1, 2, 16, 2.0)),
    }


def to_middle(matrix, inverse):
    return matrix.reshape(LO, NBLK, BLK)[:, inverse, :].reshape(LO, SEP)


def reference(leaf_mass, leaf_damp, mass_coupling, damp_coupling, leaf_modes, interface_blocks, mid_modes, mid_constraint):
    def one_group(group_id):
        eigen_modes = lax.dynamic_index_in_dim(mid_modes, group_id, 0, keepdims=False)
        root_shapes = lax.dynamic_index_in_dim(mid_constraint, group_id, 0, keepdims=False)
        mode_basis = jnp.concatenate([eigen_modes, root_shapes], axis=1)

        def one_leaf(totals, member):
            leaf_id = group_id * N_LEAF + member

            def select(stacked):
                return lax.dynamic_index_in_dim(stacked, leaf_id, 0, keepdims=False)

            inverse = jnp.argsort(select(interface_blocks)).astype(jnp.int32)
            constraint = to_middle(select(leaf_modes), inverse)
            left = jnp.dot(constraint, mode_basis, preferred_element_type=jnp.float32).astype(jnp.bfloat16)
            new_totals = []
            couplings = []
            pairs = ((select(leaf_mass), select(mass_coupling)), (select(leaf_damp), select(damp_coupling)))
            for index in range(2):
                leaf_block, side_block = pairs[index]
                side_middle = to_middle(side_block, inverse).astype(jnp.float32)
                product = jnp.dot(leaf_block, constraint, preferred_element_type=jnp.float32)
                half_work = (0.5 * product + side_middle).astype(jnp.bfloat16)
                full_work = (product + side_middle).astype(jnp.bfloat16)
                right = jnp.dot(half_work, mode_basis, preferred_element_type=jnp.float32).astype(jnp.bfloat16)
                folded = jnp.dot(left.T, right, preferred_element_type=jnp.float32)
                projected = folded + folded.T
                couplings.append(jnp.dot(full_work, eigen_modes, preferred_element_type=jnp.float32))
                new_totals.append(totals[2 * index] + projected[:MODES])
                new_totals.append(totals[2 * index + 1] + projected[MODES:, MODES:])
            return tuple(new_totals), (couplings[0], couplings[1])

        modal_zero = jnp.zeros((MODES, MODES + ROOT), jnp.float32)
        root_zero = jnp.zeros((ROOT, ROOT), jnp.float32)
        sums, couplings = lax.scan(one_leaf, (modal_zero, root_zero, modal_zero, root_zero), jnp.arange(N_LEAF, dtype=jnp.int32))
        return couplings[0], couplings[1], sums[0], sums[2], sums[1], sums[3]

    def add_group(carry, group_id):
        outs = one_group(group_id)
        return (carry[0] + outs[4], carry[1] + outs[5]), (outs[0], outs[1], outs[2], outs[3])

    root_zero = jnp.zeros((ROOT, ROOT), jnp.float32)
    roots, stacks = lax.scan(add_group, (root_zero, root_zero), jnp.arange(N_GROUP, dtype=jnp.int32))
    coupling_mass = stacks[0].reshape(LEAVES, LO, MODES)
    coupling_damp = stacks[1].reshape(LEAVES, LO, MODES)
    return (coupling_mass, coupling_damp, stacks[2], stacks[3], roots[0], roots[1])
```

```python
import jax
import jax.numpy as jnp
from jax import lax
from jax.sharding import PartitionSpec as P


def to_middle(stacked, onehot, block_count, block_size):
    rows_total, width_total = stacked.shape
    moved = jnp.einsum(
        "lbk,bj->ljk",
        stacked.reshape(rows_total, block_count, block_size),
        onehot,
        preferred_element_type=jnp.float32,
    )
    return moved.astype(jnp.bfloat16).reshape(rows_total, width_total)


def left_product(first_operand, second_operand):
    return lax.dot_general(
        first_operand, second_operand, (((0,), (0,)), ((), ())), preferred_element_type=jnp.float32
    )


def body(
    leaf_mass,
    leaf_damp,
    mass_coupling,
    damp_coupling,
    leaf_modes,
    interface_blocks,
    mid_modes,
    mid_constraint,
):
    leaf_order = leaf_mass.shape[1]
    block_count = interface_blocks.shape[1]
    sep_width = leaf_modes.shape[2]
    block_size = sep_width // block_count
    mode_count = mid_modes.shape[2]
    root_width = mid_constraint.shape[2]
    basis_width = mode_count + root_width
    leaf_count = lax.axis_size("leaf")
    group_count = lax.axis_size("group")
    onehot = (
        interface_blocks[0][:, None] == jnp.arange(block_count, dtype=jnp.int32)[None, :]
    ).astype(jnp.bfloat16)
    placed = to_middle(
        jnp.concatenate([leaf_modes[0], mass_coupling[0], damp_coupling[0]], axis=0),
        onehot,
        block_count,
        block_size,
    )
    constraint = placed[:leaf_order]
    sides = placed[leaf_order:].astype(jnp.float32)
    product = jnp.dot(
        jnp.concatenate([leaf_mass[0], leaf_damp[0]], axis=0),
        constraint,
        preferred_element_type=jnp.float32,
    )
    half_work = (0.5 * product + sides).astype(jnp.bfloat16)
    full_work = (product + sides).astype(jnp.bfloat16)
    basis_rows = jnp.concatenate([mid_modes[0], mid_constraint[0]], axis=1)
    mode_basis = lax.all_gather(basis_rows, "leaf", axis=0, tiled=True)
    left_sum = jnp.dot(constraint, mode_basis, preferred_element_type=jnp.float32)
    right_sum = jnp.dot(half_work, mode_basis, preferred_element_type=jnp.float32)
    coupling = jnp.dot(full_work, mode_basis[:, :mode_count], preferred_element_type=jnp.float32)
    left_part = left_sum.astype(jnp.bfloat16)
    right_part = right_sum.astype(jnp.bfloat16)
    right_mass = right_part[:leaf_order]
    right_damp = right_part[leaf_order:]

    def projected_rows(first_row, amount, first_col):
        left_rows = lax.dynamic_slice_in_dim(left_part, first_row, amount, 1)
        right_rows = lax.dynamic_slice_in_dim(right_part, first_row, amount, 1)
        left_cols = left_part[:, first_col:]
        mass_term = left_product(left_rows, right_mass[:, first_col:]) + left_product(
            right_rows[:leaf_order], left_cols
        )
        damp_term = left_product(left_rows, right_damp[:, first_col:]) + left_product(
            right_rows[leaf_order:], left_cols
        )
        return jnp.concatenate([mass_term, damp_term], axis=1)

    modal_part = lax.psum_scatter(
        projected_rows(jnp.int32(0), mode_count // leaf_count * lax.axis_size("leaf"), 0),
        "leaf",
        scatter_dimension=0,
        tiled=True,
    )
    root_rows = projected_rows(jnp.int32(0) + mode_count, root_width, mode_count)
    device_count = group_count * leaf_count
    root_chunks = root_rows.reshape(device_count, root_width // device_count, 2 * root_width)
    root_recv = lax.all_to_all(
        root_chunks.astype(jnp.bfloat16), ("group", "leaf"), 0, 0, tiled=True
    )
    root_part = jnp.sum(
        root_recv.reshape(device_count, root_width // device_count, 2 * root_width).astype(jnp.float32),
        axis=0,
    )
    return (
        coupling[:leaf_order][None],
        coupling[leaf_order:][None],
        modal_part[:, :basis_width][None],
        modal_part[:, basis_width:][None],
        root_part[:, :root_width],
        root_part[:, root_width:],
    )


def solution(mesh):
    return jax.shard_map(
        body,
        mesh=mesh,
        in_specs=(
            P(("group", "leaf"), None, None),
            P(("group", "leaf"), None, None),
            P(("group", "leaf"), None, None),
            P(("group", "leaf"), None, None),
            P(("group", "leaf"), None, None),
            P(("group", "leaf"), None),
            P("group", "leaf", None),
            P("group", "leaf", None),
        ),
        out_specs=(
            P(("group", "leaf"), None, None),
            P(("group", "leaf"), None, None),
            P("group", "leaf", None),
            P("group", "leaf", None),
            P(("group", "leaf"), None),
            P(("group", "leaf"), None),
        ),
        check_vma=False,
    )
```

```python
import jax
import jax.numpy as jnp
from jax import lax
from jax.sharding import PartitionSpec as P


def to_middle(stacked, onehot, block_count, block_size):
    rows_total, width_total = stacked.shape
    moved = jnp.einsum(
        "lbk,bj->ljk",
        stacked.reshape(rows_total, block_count, block_size),
        onehot,
        preferred_element_type=jnp.float32,
    )
    return moved.astype(jnp.bfloat16).reshape(rows_total, width_total)


def left_product(first_operand, second_operand):
    return lax.dot_general(
        first_operand, second_operand, (((0,), (0,)), ((), ())), preferred_element_type=jnp.float32
    )


def body(
    leaf_mass,
    leaf_damp,
    mass_coupling,
    damp_coupling,
    leaf_modes,
    interface_blocks,
    mid_modes,
    mid_constraint,
):
    leaf_order = leaf_mass.shape[1]
    block_count = interface_blocks.shape[1]
    sep_width = leaf_modes.shape[2]
    block_size = sep_width // block_count
    mode_count = mid_modes.shape[2]
    root_width = mid_constraint.shape[2]
    basis_width = mode_count + root_width
    leaf_count = lax.axis_size("leaf")
    group_count = lax.axis_size("group")
    onehot = (
        interface_blocks[0][:, None] == jnp.arange(block_count, dtype=jnp.int32)[None, :]
    ).astype(jnp.bfloat16)
    placed = to_middle(
        jnp.concatenate([leaf_modes[0], mass_coupling[0], damp_coupling[0]], axis=0),
        onehot,
        block_count,
        block_size,
    )
    constraint = placed[:leaf_order]
    sides = placed[leaf_order:].astype(jnp.float32)
    product = jnp.dot(
        jnp.concatenate([leaf_mass[0], leaf_damp[0]], axis=0),
        constraint,
        preferred_element_type=jnp.float32,
    )
    half_work = (0.5 * product + sides).astype(jnp.bfloat16)
    full_work = (product + sides).astype(jnp.bfloat16)
    basis_rows = jnp.concatenate([mid_modes[0], mid_constraint[0]], axis=1)
    mode_basis = lax.all_to_all(
        jnp.broadcast_to(basis_rows[None], (leaf_count,) + basis_rows.shape), "leaf", 0, 0, tiled=True
    ).reshape(leaf_count * basis_rows.shape[0], basis_width)
    left_sum = jnp.dot(constraint, mode_basis, preferred_element_type=jnp.float32)
    right_sum = jnp.dot(half_work, mode_basis, preferred_element_type=jnp.float32)
    coupling = jnp.dot(full_work, mode_basis[:, :mode_count], preferred_element_type=jnp.float32)
    left_part = left_sum.astype(jnp.bfloat16)
    right_part = right_sum.astype(jnp.bfloat16)
    right_mass = right_part[:leaf_order]
    right_damp = right_part[leaf_order:]

    def projected_rows(first_row, amount, first_col):
        left_rows = lax.dynamic_slice_in_dim(left_part, first_row, amount, 1)
        right_rows = lax.dynamic_slice_in_dim(right_part, first_row, amount, 1)
        left_cols = left_part[:, first_col:]
        mass_term = left_product(left_rows, right_mass[:, first_col:]) + left_product(
            right_rows[:leaf_order], left_cols
        )
        damp_term = left_product(left_rows, right_damp[:, first_col:]) + left_product(
            right_rows[leaf_order:], left_cols
        )
        return jnp.concatenate([mass_term, damp_term], axis=1)

    modal_part = lax.psum_scatter(
        projected_rows(jnp.int32(0), mode_count // leaf_count * lax.axis_size("leaf"), 0),
        "leaf",
        scatter_dimension=0,
        tiled=True,
    )
    root_rows = projected_rows(jnp.int32(0) + mode_count, root_width, mode_count)
    device_count = group_count * leaf_count
    root_chunks = root_rows.reshape(device_count, root_width // device_count, 2 * root_width)
    root_recv = lax.all_to_all(
        root_chunks.astype(jnp.bfloat16), ("group", "leaf"), 0, 0, tiled=True
    )
    root_part = jnp.sum(
        root_recv.reshape(device_count, root_width // device_count, 2 * root_width).astype(jnp.float32),
        axis=0,
    )
    return (
        coupling[:leaf_order][None],
        coupling[leaf_order:][None],
        modal_part[:, :basis_width][None],
        modal_part[:, basis_width:][None],
        root_part[:, :root_width],
        root_part[:, root_width:],
    )


def solution(mesh):
    return jax.shard_map(
        body,
        mesh=mesh,
        in_specs=(
            P(("group", "leaf"), None, None),
            P(("group", "leaf"), None, None),
            P(("group", "leaf"), None, None),
            P(("group", "leaf"), None, None),
            P(("group", "leaf"), None, None),
            P(("group", "leaf"), None),
            P("group", "leaf", None),
            P("group", "leaf", None),
        ),
        out_specs=(
            P(("group", "leaf"), None, None),
            P(("group", "leaf"), None, None),
            P("group", "leaf", None),
            P("group", "leaf", None),
            P(("group", "leaf"), None),
            P(("group", "leaf"), None),
        ),
        check_vma=False,
    )
```

```python
import jax
import jax.numpy as jnp
from jax import lax
from jax.sharding import PartitionSpec as P


def to_middle(stacked, onehot, block_count, block_size):
    rows_total, width_total = stacked.shape
    moved = jnp.einsum(
        "lbk,bj->ljk",
        stacked.reshape(rows_total, block_count, block_size),
        onehot,
        preferred_element_type=jnp.float32,
    )
    return moved.astype(jnp.bfloat16).reshape(rows_total, width_total)


def left_product(first_operand, second_operand):
    return lax.dot_general(
        first_operand, second_operand, (((0,), (0,)), ((), ())), preferred_element_type=jnp.float32
    )


def body(
    leaf_mass,
    leaf_damp,
    mass_coupling,
    damp_coupling,
    leaf_modes,
    interface_blocks,
    mid_modes,
    mid_constraint,
):
    leaf_order = leaf_mass.shape[1]
    block_count = interface_blocks.shape[1]
    sep_width = leaf_modes.shape[2]
    block_size = sep_width // block_count
    mode_count = mid_modes.shape[2]
    root_width = mid_constraint.shape[2]
    basis_width = mode_count + root_width
    leaf_count = lax.axis_size("leaf")
    group_count = lax.axis_size("group")
    onehot = (
        interface_blocks[0][:, None] == jnp.arange(block_count, dtype=jnp.int32)[None, :]
    ).astype(jnp.bfloat16)
    placed = to_middle(
        jnp.concatenate([leaf_modes[0], mass_coupling[0], damp_coupling[0]], axis=0),
        onehot,
        block_count,
        block_size,
    )
    constraint = placed[:leaf_order]
    sides = placed[leaf_order:].astype(jnp.float32)
    product = jnp.dot(
        jnp.concatenate([leaf_mass[0], leaf_damp[0]], axis=0),
        constraint,
        preferred_element_type=jnp.float32,
    )
    half_work = (0.5 * product + sides).astype(jnp.bfloat16)
    full_work = (product + sides).astype(jnp.bfloat16)
    basis_rows = jnp.concatenate([mid_modes[0], mid_constraint[0]], axis=1)
    mode_basis = lax.all_gather(basis_rows, "leaf", axis=0, tiled=True)
    left_sum = jnp.dot(constraint, mode_basis, preferred_element_type=jnp.float32)
    right_sum = jnp.dot(half_work, mode_basis, preferred_element_type=jnp.float32)
    coupling = jnp.dot(full_work, mode_basis[:, :mode_count], preferred_element_type=jnp.float32)
    left_part = left_sum.astype(jnp.bfloat16)
    right_part = right_sum.astype(jnp.bfloat16)
    right_mass = right_part[:leaf_order]
    right_damp = right_part[leaf_order:]

    def projected_rows(first_row, amount, first_col):
        left_rows = lax.dynamic_slice_in_dim(left_part, first_row, amount, 1)
        right_rows = lax.dynamic_slice_in_dim(right_part, first_row, amount, 1)
        left_cols = left_part[:, first_col:]
        mass_term = left_product(left_rows, right_mass[:, first_col:]) + left_product(
            right_rows[:leaf_order], left_cols
        )
        damp_term = left_product(left_rows, right_damp[:, first_col:]) + left_product(
            right_rows[leaf_order:], left_cols
        )
        return jnp.concatenate([mass_term, damp_term], axis=1)

    modal_rows = projected_rows(jnp.int32(0), mode_count, 0)
    modal_recv = lax.all_to_all(
        modal_rows.reshape(leaf_count, mode_count // leaf_count, 2 * basis_width).astype(jnp.bfloat16),
        "leaf",
        0,
        0,
        tiled=True,
    )
    modal_part = jnp.sum(
        modal_recv.reshape(leaf_count, mode_count // leaf_count, 2 * basis_width).astype(jnp.float32),
        axis=0,
    )
    root_rows = projected_rows(jnp.int32(0) + mode_count, root_width, mode_count)
    device_count = group_count * leaf_count
    root_chunks = root_rows.reshape(device_count, root_width // device_count, 2 * root_width)
    root_recv = lax.all_to_all(
        root_chunks.astype(jnp.bfloat16), ("group", "leaf"), 0, 0, tiled=True
    )
    root_part = jnp.sum(
        root_recv.reshape(device_count, root_width // device_count, 2 * root_width).astype(jnp.float32),
        axis=0,
    )
    return (
        coupling[:leaf_order][None],
        coupling[leaf_order:][None],
        modal_part[:, :basis_width][None],
        modal_part[:, basis_width:][None],
        root_part[:, :root_width],
        root_part[:, root_width:],
    )


def solution(mesh):
    return jax.shard_map(
        body,
        mesh=mesh,
        in_specs=(
            P(("group", "leaf"), None, None),
            P(("group", "leaf"), None, None),
            P(("group", "leaf"), None, None),
            P(("group", "leaf"), None, None),
            P(("group", "leaf"), None, None),
            P(("group", "leaf"), None),
            P("group", "leaf", None),
            P("group", "leaf", None),
        ),
        out_specs=(
            P(("group", "leaf"), None, None),
            P(("group", "leaf"), None, None),
            P("group", "leaf", None),
            P("group", "leaf", None),
            P(("group", "leaf"), None),
            P(("group", "leaf"), None),
        ),
        check_vma=False,
    )
```

```python
import jax
import jax.numpy as jnp
from jax import lax
from jax.sharding import PartitionSpec as P


def to_middle(stacked, onehot, block_count, block_size):
    rows_total, width_total = stacked.shape
    moved = jnp.einsum(
        "lbk,bj->ljk",
        stacked.reshape(rows_total, block_count, block_size),
        onehot,
        preferred_element_type=jnp.float32,
    )
    return moved.astype(jnp.bfloat16).reshape(rows_total, width_total)


def left_product(first_operand, second_operand):
    return lax.dot_general(
        first_operand, second_operand, (((0,), (0,)), ((), ())), preferred_element_type=jnp.float32
    )


def body(
    leaf_mass,
    leaf_damp,
    mass_coupling,
    damp_coupling,
    leaf_modes,
    interface_blocks,
    mid_modes,
    mid_constraint,
):
    leaf_order = leaf_mass.shape[1]
    block_count = interface_blocks.shape[1]
    sep_width = leaf_modes.shape[2]
    block_size = sep_width // block_count
    mode_count = mid_modes.shape[2]
    root_width = mid_constraint.shape[2]
    basis_width = mode_count + root_width
    leaf_count = lax.axis_size("leaf")
    group_count = lax.axis_size("group")
    onehot = (
        interface_blocks[0][:, None] == jnp.arange(block_count, dtype=jnp.int32)[None, :]
    ).astype(jnp.bfloat16)
    placed = to_middle(
        jnp.concatenate([leaf_modes[0], mass_coupling[0], damp_coupling[0]], axis=0),
        onehot,
        block_count,
        block_size,
    )
    constraint = placed[:leaf_order]
    sides = placed[leaf_order:].astype(jnp.float32)
    product = jnp.dot(
        jnp.concatenate([leaf_mass[0], leaf_damp[0]], axis=0),
        constraint,
        preferred_element_type=jnp.float32,
    )
    half_work = (0.5 * product + sides).astype(jnp.bfloat16)
    full_work = (product + sides).astype(jnp.bfloat16)
    basis_rows = jnp.concatenate([mid_modes[0], mid_constraint[0]], axis=1)
    mode_basis = lax.all_gather(basis_rows, "leaf", axis=0, tiled=True)
    left_sum = jnp.dot(constraint, mode_basis, preferred_element_type=jnp.float32)
    right_sum = jnp.dot(half_work, mode_basis, preferred_element_type=jnp.float32)
    coupling = jnp.dot(full_work, mode_basis[:, :mode_count], preferred_element_type=jnp.float32)
    left_part = left_sum.astype(jnp.bfloat16)
    right_part = right_sum.astype(jnp.bfloat16)
    right_mass = right_part[:leaf_order]
    right_damp = right_part[leaf_order:]

    def projected_rows(first_row, amount, first_col):
        left_rows = lax.dynamic_slice_in_dim(left_part, first_row, amount, 1)
        right_rows = lax.dynamic_slice_in_dim(right_part, first_row, amount, 1)
        left_cols = left_part[:, first_col:]
        mass_term = left_product(left_rows, right_mass[:, first_col:]) + left_product(
            right_rows[:leaf_order], left_cols
        )
        damp_term = left_product(left_rows, right_damp[:, first_col:]) + left_product(
            right_rows[leaf_order:], left_cols
        )
        return jnp.concatenate([mass_term, damp_term], axis=1)

    modal_rows = projected_rows(jnp.int32(0), mode_count, 0)
    modal_recv = lax.all_to_all(
        modal_rows.reshape(leaf_count, mode_count // leaf_count, 2 * basis_width).astype(jnp.bfloat16),
        "leaf",
        0,
        0,
        tiled=True,
    )
    modal_part = jnp.sum(
        modal_recv.reshape(leaf_count, mode_count // leaf_count, 2 * basis_width).astype(jnp.float32),
        axis=0,
    )
    device_count = group_count * leaf_count
    core_odd = lax.axis_index("group") % 2 == 1
    left_root = left_part[:, mode_count:]
    mass_root = right_mass[:, mode_count:]
    damp_root = right_damp[:, mode_count:]
    own_right = jnp.where(core_odd, damp_root, mass_root)
    other_right = jnp.where(core_odd, mass_root, damp_root)
    partner = lax.ppermute(
        jnp.concatenate([left_root, other_right], axis=0),
        "group",
        [(index, index ^ 1) for index in range(group_count)],
    )
    left_pair = jnp.concatenate([left_root, partner[:leaf_order]], axis=0)
    right_pair = jnp.concatenate([own_right, partner[leaf_order:]], axis=0)
    root_rows = left_product(left_pair, right_pair) + left_product(right_pair, left_pair)
    root_recv = lax.all_to_all(
        root_rows.reshape(device_count, root_width // device_count, root_width).astype(jnp.bfloat16),
        ("group", "leaf"),
        0,
        0,
        tiled=True,
    )
    root_part = jnp.sum(
        root_recv.reshape(
            group_count // 2, 2, leaf_count, root_width // device_count, root_width
        ).astype(jnp.float32),
        axis=(0, 2),
    )
    return (
        coupling[:leaf_order][None],
        coupling[leaf_order:][None],
        modal_part[:, :basis_width][None],
        modal_part[:, basis_width:][None],
        root_part[0],
        root_part[1],
    )


def solution(mesh):
    return jax.shard_map(
        body,
        mesh=mesh,
        in_specs=(
            P(("group", "leaf"), None, None),
            P(("group", "leaf"), None, None),
            P(("group", "leaf"), None, None),
            P(("group", "leaf"), None, None),
            P(("group", "leaf"), None, None),
            P(("group", "leaf"), None),
            P("group", "leaf", None),
            P("group", "leaf", None),
        ),
        out_specs=(
            P(("group", "leaf"), None, None),
            P(("group", "leaf"), None, None),
            P("group", "leaf", None),
            P("group", "leaf", None),
            P(("group", "leaf"), None),
            P(("group", "leaf"), None),
        ),
        check_vma=False,
    )
```

```python
import jax
import jax.numpy as jnp
from jax import lax
from jax.sharding import PartitionSpec as P


def to_middle(stacked, onehot, block_count, block_size):
    rows_total, width_total = stacked.shape
    moved = jnp.einsum(
        "lbk,bj->ljk",
        stacked.reshape(rows_total, block_count, block_size),
        onehot,
        preferred_element_type=jnp.float32,
    )
    return moved.astype(jnp.bfloat16).reshape(rows_total, width_total)


def left_product(first_operand, second_operand):
    return lax.dot_general(
        first_operand, second_operand, (((0,), (0,)), ((), ())), preferred_element_type=jnp.float32
    )


def gather_leaf(rows, leaf_count):
    ring = leaf_count // 2
    own = lax.axis_index("leaf")
    upper = own // ring
    other = lax.ppermute(rows, "leaf", [(i, (i + ring) % leaf_count) for i in range(leaf_count)])
    pair = jnp.stack([jnp.where(upper == 0, rows, other), jnp.where(upper == 0, other, rows)])
    ahead = [(i, (i // ring) * ring + (i % ring + 1) % ring) for i in range(leaf_count)]
    behind = [(i, (i // ring) * ring + (i % ring - 1) % ring) for i in range(leaf_count)]
    from_behind = []
    from_ahead = []
    forward = pair
    backward = pair
    for step in range(1, ring // 2 + 1):
        forward = lax.ppermute(forward, "leaf", ahead)
        from_behind.append(forward)
        if step < ring - ring // 2:
            backward = lax.ppermute(backward, "leaf", behind)
            from_ahead.append(backward)
    relative = jnp.stack([pair] + from_ahead + from_behind[::-1])
    placed = jnp.roll(relative, own % ring, axis=0)
    return jnp.swapaxes(placed, 0, 1).reshape(leaf_count * rows.shape[0], rows.shape[1])


def body(
    leaf_mass,
    leaf_damp,
    mass_coupling,
    damp_coupling,
    leaf_modes,
    interface_blocks,
    mid_modes,
    mid_constraint,
):
    leaf_order = leaf_mass.shape[1]
    block_count = interface_blocks.shape[1]
    sep_width = leaf_modes.shape[2]
    block_size = sep_width // block_count
    mode_count = mid_modes.shape[2]
    root_width = mid_constraint.shape[2]
    basis_width = mode_count + root_width
    leaf_count = lax.axis_size("leaf")
    group_count = lax.axis_size("group")
    onehot = (
        interface_blocks[0][:, None] == jnp.arange(block_count, dtype=jnp.int32)[None, :]
    ).astype(jnp.bfloat16)
    placed = to_middle(
        jnp.concatenate([leaf_modes[0], mass_coupling[0], damp_coupling[0]], axis=0),
        onehot,
        block_count,
        block_size,
    )
    constraint = placed[:leaf_order]
    sides = placed[leaf_order:].astype(jnp.float32)
    product = jnp.dot(
        jnp.concatenate([leaf_mass[0], leaf_damp[0]], axis=0),
        constraint,
        preferred_element_type=jnp.float32,
    )
    half_work = (0.5 * product + sides).astype(jnp.bfloat16)
    full_work = (product + sides).astype(jnp.bfloat16)
    basis_rows = jnp.concatenate([mid_modes[0], mid_constraint[0]], axis=1)
    mode_basis = gather_leaf(basis_rows, leaf_count)
    left_sum = jnp.dot(constraint, mode_basis, preferred_element_type=jnp.float32)
    right_sum = jnp.dot(half_work, mode_basis, preferred_element_type=jnp.float32)
    coupling = jnp.dot(full_work, mode_basis[:, :mode_count], preferred_element_type=jnp.float32)
    left_part = left_sum.astype(jnp.bfloat16)
    right_part = right_sum.astype(jnp.bfloat16)
    right_mass = right_part[:leaf_order]
    right_damp = right_part[leaf_order:]

    def projected_rows(first_row, amount, first_col):
        left_rows = lax.dynamic_slice_in_dim(left_part, first_row, amount, 1)
        right_rows = lax.dynamic_slice_in_dim(right_part, first_row, amount, 1)
        left_cols = left_part[:, first_col:]
        mass_term = left_product(left_rows, right_mass[:, first_col:]) + left_product(
            right_rows[:leaf_order], left_cols
        )
        damp_term = left_product(left_rows, right_damp[:, first_col:]) + left_product(
            right_rows[leaf_order:], left_cols
        )
        return jnp.concatenate([mass_term, damp_term], axis=1)

    modal_rows = projected_rows(jnp.int32(0), mode_count, 0)
    modal_recv = lax.all_to_all(
        modal_rows.reshape(leaf_count, mode_count // leaf_count, 2 * basis_width).astype(jnp.bfloat16),
        "leaf",
        0,
        0,
        tiled=True,
    )
    modal_part = jnp.sum(
        modal_recv.reshape(leaf_count, mode_count // leaf_count, 2 * basis_width).astype(jnp.float32),
        axis=0,
    )
    device_count = group_count * leaf_count
    core_odd = lax.axis_index("group") % 2 == 1
    left_root = left_part[:, mode_count:]
    mass_root = right_mass[:, mode_count:]
    damp_root = right_damp[:, mode_count:]
    own_right = jnp.where(core_odd, damp_root, mass_root)
    other_right = jnp.where(core_odd, mass_root, damp_root)
    partner = lax.ppermute(
        jnp.concatenate([left_root, other_right], axis=0),
        "group",
        [(index, index ^ 1) for index in range(group_count)],
    )
    left_pair = jnp.concatenate([left_root, partner[:leaf_order]], axis=0)
    right_pair = jnp.concatenate([own_right, partner[leaf_order:]], axis=0)
    root_rows = left_product(left_pair, right_pair) + left_product(right_pair, left_pair)
    root_recv = lax.all_to_all(
        root_rows.reshape(device_count, root_width // device_count, root_width).astype(jnp.bfloat16),
        ("group", "leaf"),
        0,
        0,
        tiled=True,
    )
    root_part = jnp.sum(
        root_recv.reshape(
            group_count // 2, 2, leaf_count, root_width // device_count, root_width
        ).astype(jnp.float32),
        axis=(0, 2),
    )
    return (
        coupling[:leaf_order][None],
        coupling[leaf_order:][None],
        modal_part[:, :basis_width][None],
        modal_part[:, basis_width:][None],
        root_part[0],
        root_part[1],
    )


def solution(mesh):
    return jax.shard_map(
        body,
        mesh=mesh,
        in_specs=(
            P(("group", "leaf"), None, None),
            P(("group", "leaf"), None, None),
            P(("group", "leaf"), None, None),
            P(("group", "leaf"), None, None),
            P(("group", "leaf"), None, None),
            P(("group", "leaf"), None),
            P("group", "leaf", None),
            P("group", "leaf", None),
        ),
        out_specs=(
            P(("group", "leaf"), None, None),
            P(("group", "leaf"), None, None),
            P("group", "leaf", None),
            P("group", "leaf", None),
            P(("group", "leaf"), None),
            P(("group", "leaf"), None),
        ),
        check_vma=False,
    )
```

```python
import jax
import jax.numpy as jnp
from jax import lax
from jax.sharding import PartitionSpec as P


def to_middle(stacked, onehot, block_count, block_size):
    rows_total, width_total = stacked.shape
    moved = jnp.einsum(
        "lbk,bj->ljk",
        stacked.reshape(rows_total, block_count, block_size),
        onehot,
        preferred_element_type=jnp.float32,
    )
    return moved.astype(jnp.bfloat16).reshape(rows_total, width_total)


def left_product(first_operand, second_operand):
    return lax.dot_general(
        first_operand, second_operand, (((0,), (0,)), ((), ())), preferred_element_type=jnp.float32
    )


def body(
    leaf_mass,
    leaf_damp,
    mass_coupling,
    damp_coupling,
    leaf_modes,
    interface_blocks,
    mid_modes,
    mid_constraint,
):
    leaf_order = leaf_mass.shape[1]
    block_count = interface_blocks.shape[1]
    sep_width = leaf_modes.shape[2]
    block_size = sep_width // block_count
    mode_count = mid_modes.shape[2]
    root_width = mid_constraint.shape[2]
    basis_width = mode_count + root_width
    leaf_count = lax.axis_size("leaf")
    group_count = lax.axis_size("group")
    onehot = (
        interface_blocks[0][:, None] == jnp.arange(block_count, dtype=jnp.int32)[None, :]
    ).astype(jnp.bfloat16)
    placed = to_middle(
        jnp.concatenate([leaf_modes[0], mass_coupling[0], damp_coupling[0]], axis=0),
        onehot,
        block_count,
        block_size,
    )
    constraint = placed[:leaf_order]
    sides = placed[leaf_order:].astype(jnp.float32)
    product = jnp.dot(
        jnp.concatenate([leaf_mass[0], leaf_damp[0]], axis=0),
        constraint,
        preferred_element_type=jnp.float32,
    )
    half_work = (0.5 * product + sides).astype(jnp.bfloat16)
    full_work = (product + sides).astype(jnp.bfloat16)
    basis_rows = jnp.concatenate([mid_modes[0], mid_constraint[0]], axis=1)
    mode_basis = lax.all_gather(basis_rows, "leaf", axis=0, tiled=True)
    left_sum = jnp.dot(constraint, mode_basis, preferred_element_type=jnp.float32)
    right_sum = jnp.dot(half_work, mode_basis, preferred_element_type=jnp.float32)
    coupling = jnp.dot(full_work, mode_basis[:, :mode_count], preferred_element_type=jnp.float32)
    left_part = left_sum.astype(jnp.bfloat16)
    right_part = right_sum.astype(jnp.bfloat16)
    right_mass = right_part[:leaf_order]
    right_damp = right_part[leaf_order:]

    def projected_rows(first_row, amount, first_col):
        left_rows = lax.dynamic_slice_in_dim(left_part, first_row, amount, 1)
        right_rows = lax.dynamic_slice_in_dim(right_part, first_row, amount, 1)
        left_cols = left_part[:, first_col:]
        mass_term = left_product(left_rows, right_mass[:, first_col:]) + left_product(
            right_rows[:leaf_order], left_cols
        )
        damp_term = left_product(left_rows, right_damp[:, first_col:]) + left_product(
            right_rows[leaf_order:], left_cols
        )
        return jnp.concatenate([mass_term, damp_term], axis=1)

    modal_part = lax.psum_scatter(
        projected_rows(jnp.int32(0), mode_count, 0), "leaf", scatter_dimension=0, tiled=True
    )
    device_count = group_count * leaf_count
    core_odd = lax.axis_index("group") % 2 == 1
    left_root = left_part[:, mode_count:]
    mass_root = right_mass[:, mode_count:]
    damp_root = right_damp[:, mode_count:]
    own_right = jnp.where(core_odd, damp_root, mass_root)
    other_right = jnp.where(core_odd, mass_root, damp_root)
    partner = lax.ppermute(
        jnp.concatenate([left_root, other_right], axis=0),
        "group",
        [(index, index ^ 1) for index in range(group_count)],
    )
    left_pair = jnp.concatenate([left_root, partner[:leaf_order]], axis=0)
    right_pair = jnp.concatenate([own_right, partner[leaf_order:]], axis=0)
    root_rows = left_product(left_pair, right_pair) + left_product(right_pair, left_pair)
    root_recv = lax.all_to_all(
        root_rows.reshape(device_count, root_width // device_count, root_width).astype(jnp.bfloat16),
        ("group", "leaf"),
        0,
        0,
        tiled=True,
    )
    root_part = jnp.sum(
        root_recv.reshape(
            group_count // 2, 2, leaf_count, root_width // device_count, root_width
        ).astype(jnp.float32),
        axis=(0, 2),
    )
    return (
        coupling[:leaf_order][None],
        coupling[leaf_order:][None],
        modal_part[:, :basis_width][None],
        modal_part[:, basis_width:][None],
        root_part[0],
        root_part[1],
    )


def solution(mesh):
    return jax.shard_map(
        body,
        mesh=mesh,
        in_specs=(
            P(("group", "leaf"), None, None),
            P(("group", "leaf"), None, None),
            P(("group", "leaf"), None, None),
            P(("group", "leaf"), None, None),
            P(("group", "leaf"), None, None),
            P(("group", "leaf"), None),
            P("group", "leaf", None),
            P("group", "leaf", None),
        ),
        out_specs=(
            P(("group", "leaf"), None, None),
            P(("group", "leaf"), None, None),
            P("group", "leaf", None),
            P("group", "leaf", None),
            P(("group", "leaf"), None),
            P(("group", "leaf"), None),
        ),
        check_vma=False,
    )
```

```python
import jax
import jax.numpy as jnp
from jax import lax
from jax.sharding import PartitionSpec as P


def to_middle(stacked, onehot, block_count, block_size):
    rows_total, width_total = stacked.shape
    moved = jnp.einsum(
        "lbk,bj->ljk",
        stacked.reshape(rows_total, block_count, block_size),
        onehot,
        preferred_element_type=jnp.float32,
    )
    return moved.astype(jnp.bfloat16).reshape(rows_total, width_total)


def left_product(first_operand, second_operand):
    return lax.dot_general(
        first_operand, second_operand, (((0,), (0,)), ((), ())), preferred_element_type=jnp.float32
    )


def gather_leaf(rows, leaf_count):
    ring = leaf_count // 2
    own = lax.axis_index("leaf")
    upper = own // ring
    other = lax.ppermute(rows, "leaf", [(i, (i + ring) % leaf_count) for i in range(leaf_count)])
    pair = jnp.stack([jnp.where(upper == 0, rows, other), jnp.where(upper == 0, other, rows)])
    ahead = [(i, (i // ring) * ring + (i % ring + 1) % ring) for i in range(leaf_count)]
    behind = [(i, (i // ring) * ring + (i % ring - 1) % ring) for i in range(leaf_count)]
    from_behind = []
    from_ahead = []
    forward = pair
    backward = pair
    for step in range(1, ring // 2 + 1):
        forward = lax.ppermute(forward, "leaf", ahead)
        from_behind.append(forward)
        if step < ring - ring // 2:
            backward = lax.ppermute(backward, "leaf", behind)
            from_ahead.append(backward)
    relative = jnp.stack([pair] + from_ahead + from_behind[::-1])
    placed = jnp.roll(relative, own % ring, axis=0)
    return jnp.swapaxes(placed, 0, 1).reshape(leaf_count * rows.shape[0], rows.shape[1])


def body(
    leaf_mass,
    leaf_damp,
    mass_coupling,
    damp_coupling,
    leaf_modes,
    interface_blocks,
    mid_modes,
    mid_constraint,
):
    leaf_order = leaf_mass.shape[1]
    block_count = interface_blocks.shape[1]
    sep_width = leaf_modes.shape[2]
    block_size = sep_width // block_count
    mode_count = mid_modes.shape[2]
    root_width = mid_constraint.shape[2]
    basis_width = mode_count + root_width
    leaf_count = lax.axis_size("leaf")
    group_count = lax.axis_size("group")
    onehot = (
        interface_blocks[0][:, None] == jnp.arange(block_count, dtype=jnp.int32)[None, :]
    ).astype(jnp.bfloat16)
    placed = to_middle(
        jnp.concatenate([leaf_modes[0], mass_coupling[0], damp_coupling[0]], axis=0),
        onehot,
        block_count,
        block_size,
    )
    constraint = placed[:leaf_order]
    sides = placed[leaf_order:].astype(jnp.float32)
    product = jnp.dot(
        jnp.concatenate([leaf_mass[0], leaf_damp[0]], axis=0),
        constraint,
        preferred_element_type=jnp.float32,
    )
    half_work = (0.5 * product + sides).astype(jnp.bfloat16)
    full_work = (product + sides).astype(jnp.bfloat16)
    basis_rows = jnp.concatenate([mid_modes[0], mid_constraint[0]], axis=1)
    split_at = basis_width // 2
    mode_basis = jnp.concatenate(
        [
            lax.all_gather(basis_rows[:, :split_at], "leaf", axis=0, tiled=True),
            gather_leaf(basis_rows[:, split_at:], leaf_count),
        ],
        axis=1,
    )
    left_sum = jnp.dot(constraint, mode_basis, preferred_element_type=jnp.float32)
    right_sum = jnp.dot(half_work, mode_basis, preferred_element_type=jnp.float32)
    coupling = jnp.dot(full_work, mode_basis[:, :mode_count], preferred_element_type=jnp.float32)
    left_part = left_sum.astype(jnp.bfloat16)
    right_part = right_sum.astype(jnp.bfloat16)
    right_mass = right_part[:leaf_order]
    right_damp = right_part[leaf_order:]

    def projected_rows(first_row, amount, first_col):
        left_rows = lax.dynamic_slice_in_dim(left_part, first_row, amount, 1)
        right_rows = lax.dynamic_slice_in_dim(right_part, first_row, amount, 1)
        left_cols = left_part[:, first_col:]
        mass_term = left_product(left_rows, right_mass[:, first_col:]) + left_product(
            right_rows[:leaf_order], left_cols
        )
        damp_term = left_product(left_rows, right_damp[:, first_col:]) + left_product(
            right_rows[leaf_order:], left_cols
        )
        return jnp.concatenate([mass_term, damp_term], axis=1)

    modal_part = lax.psum_scatter(
        projected_rows(jnp.int32(0), mode_count, 0), "leaf", scatter_dimension=0, tiled=True
    )
    device_count = group_count * leaf_count
    core_odd = lax.axis_index("group") % 2 == 1
    left_root = left_part[:, mode_count:]
    mass_root = right_mass[:, mode_count:]
    damp_root = right_damp[:, mode_count:]
    own_right = jnp.where(core_odd, damp_root, mass_root)
    other_right = jnp.where(core_odd, mass_root, damp_root)
    partner = lax.ppermute(
        jnp.concatenate([left_root, other_right], axis=0),
        "group",
        [(index, index ^ 1) for index in range(group_count)],
    )
    left_pair = jnp.concatenate([left_root, partner[:leaf_order]], axis=0)
    right_pair = jnp.concatenate([own_right, partner[leaf_order:]], axis=0)
    root_rows = left_product(left_pair, right_pair) + left_product(right_pair, left_pair)
    root_recv = lax.all_to_all(
        root_rows.reshape(device_count, root_width // device_count, root_width).astype(jnp.bfloat16),
        ("group", "leaf"),
        0,
        0,
        tiled=True,
    )
    root_part = jnp.sum(
        root_recv.reshape(
            group_count // 2, 2, leaf_count, root_width // device_count, root_width
        ).astype(jnp.float32),
        axis=(0, 2),
    )
    return (
        coupling[:leaf_order][None],
        coupling[leaf_order:][None],
        modal_part[:, :basis_width][None],
        modal_part[:, basis_width:][None],
        root_part[0],
        root_part[1],
    )


def solution(mesh):
    return jax.shard_map(
        body,
        mesh=mesh,
        in_specs=(
            P(("group", "leaf"), None, None),
            P(("group", "leaf"), None, None),
            P(("group", "leaf"), None, None),
            P(("group", "leaf"), None, None),
            P(("group", "leaf"), None, None),
            P(("group", "leaf"), None),
            P("group", "leaf", None),
            P("group", "leaf", None),
        ),
        out_specs=(
            P(("group", "leaf"), None, None),
            P(("group", "leaf"), None, None),
            P("group", "leaf", None),
            P("group", "leaf", None),
            P(("group", "leaf"), None),
            P(("group", "leaf"), None),
        ),
        check_vma=False,
    )
```

```python
import jax
import jax.numpy as jnp
from jax import lax
from jax.sharding import PartitionSpec as P


def to_middle(stacked, onehot, block_count, block_size):
    rows_total, width_total = stacked.shape
    moved = jnp.einsum(
        "lbk,bj->ljk",
        stacked.reshape(rows_total, block_count, block_size),
        onehot,
        preferred_element_type=jnp.float32,
    )
    return moved.astype(jnp.bfloat16).reshape(rows_total, width_total)


def left_product(first_operand, second_operand):
    return lax.dot_general(
        first_operand, second_operand, (((0,), (0,)), ((), ())), preferred_element_type=jnp.float32
    )


def body(
    leaf_mass,
    leaf_damp,
    mass_coupling,
    damp_coupling,
    leaf_modes,
    interface_blocks,
    mid_modes,
    mid_constraint,
):
    leaf_order = leaf_mass.shape[1]
    block_count = interface_blocks.shape[1]
    sep_width = leaf_modes.shape[2]
    block_size = sep_width // block_count
    mode_count = mid_modes.shape[2]
    root_width = mid_constraint.shape[2]
    basis_width = mode_count + root_width
    leaf_count = lax.axis_size("leaf")
    group_count = lax.axis_size("group")
    onehot = (
        interface_blocks[0][:, None] == jnp.arange(block_count, dtype=jnp.int32)[None, :]
    ).astype(jnp.bfloat16)
    placed = to_middle(
        jnp.concatenate([leaf_modes[0], mass_coupling[0], damp_coupling[0]], axis=0),
        onehot,
        block_count,
        block_size,
    )
    constraint = placed[:leaf_order]
    sides = placed[leaf_order:].astype(jnp.float32)
    product = jnp.dot(
        jnp.concatenate([leaf_mass[0], leaf_damp[0]], axis=0),
        constraint,
        preferred_element_type=jnp.float32,
    )
    half_work = (0.5 * product + sides).astype(jnp.bfloat16)
    full_work = (product + sides).astype(jnp.bfloat16)
    basis_rows = jnp.concatenate([mid_modes[0], mid_constraint[0]], axis=1)
    mode_basis = lax.all_gather(basis_rows, "leaf", axis=0, tiled=True)
    left_sum = jnp.dot(constraint, mode_basis, preferred_element_type=jnp.float32)
    right_sum = jnp.dot(half_work, mode_basis, preferred_element_type=jnp.float32)
    coupling = jnp.dot(full_work, mode_basis[:, :mode_count], preferred_element_type=jnp.float32)
    left_part = left_sum.astype(jnp.bfloat16)
    right_part = right_sum.astype(jnp.bfloat16)
    right_mass = right_part[:leaf_order]
    right_damp = right_part[leaf_order:]

    def projected_rows(first_row, amount, first_col):
        left_rows = lax.dynamic_slice_in_dim(left_part, first_row, amount, 1)
        right_rows = lax.dynamic_slice_in_dim(right_part, first_row, amount, 1)
        left_cols = left_part[:, first_col:]
        mass_term = left_product(left_rows, right_mass[:, first_col:]) + left_product(
            right_rows[:leaf_order], left_cols
        )
        damp_term = left_product(left_rows, right_damp[:, first_col:]) + left_product(
            right_rows[leaf_order:], left_cols
        )
        return jnp.concatenate([mass_term, damp_term], axis=1)

    modal_rows = projected_rows(jnp.int32(0), mode_count, 0)
    kept_width = basis_width + mode_count
    modal_kept = lax.psum_scatter(modal_rows[:, :kept_width], "leaf", scatter_dimension=0, tiled=True)
    modal_sent = lax.all_to_all(
        modal_rows[:, kept_width:]
        .reshape(leaf_count, mode_count // leaf_count, 2 * basis_width - kept_width)
        .astype(jnp.bfloat16),
        "leaf",
        0,
        0,
        tiled=True,
    )
    modal_part = jnp.concatenate(
        [
            modal_kept,
            jnp.sum(
                modal_sent.reshape(
                    leaf_count, mode_count // leaf_count, 2 * basis_width - kept_width
                ).astype(jnp.float32),
                axis=0,
            ),
        ],
        axis=1,
    )
    device_count = group_count * leaf_count
    core_odd = lax.axis_index("group") % 2 == 1
    left_root = left_part[:, mode_count:]
    mass_root = right_mass[:, mode_count:]
    damp_root = right_damp[:, mode_count:]
    own_right = jnp.where(core_odd, damp_root, mass_root)
    other_right = jnp.where(core_odd, mass_root, damp_root)
    partner = lax.ppermute(
        jnp.concatenate([left_root, other_right], axis=0),
        "group",
        [(index, index ^ 1) for index in range(group_count)],
    )
    left_pair = jnp.concatenate([left_root, partner[:leaf_order]], axis=0)
    right_pair = jnp.concatenate([own_right, partner[leaf_order:]], axis=0)
    root_rows = left_product(left_pair, right_pair) + left_product(right_pair, left_pair)
    root_recv = lax.all_to_all(
        root_rows.reshape(device_count, root_width // device_count, root_width).astype(jnp.bfloat16),
        ("group", "leaf"),
        0,
        0,
        tiled=True,
    )
    root_part = jnp.sum(
        root_recv.reshape(
            group_count // 2, 2, leaf_count, root_width // device_count, root_width
        ).astype(jnp.float32),
        axis=(0, 2),
    )
    return (
        coupling[:leaf_order][None],
        coupling[leaf_order:][None],
        modal_part[:, :basis_width][None],
        modal_part[:, basis_width:][None],
        root_part[0],
        root_part[1],
    )


def solution(mesh):
    return jax.shard_map(
        body,
        mesh=mesh,
        in_specs=(
            P(("group", "leaf"), None, None),
            P(("group", "leaf"), None, None),
            P(("group", "leaf"), None, None),
            P(("group", "leaf"), None, None),
            P(("group", "leaf"), None, None),
            P(("group", "leaf"), None),
            P("group", "leaf", None),
            P("group", "leaf", None),
        ),
        out_specs=(
            P(("group", "leaf"), None, None),
            P(("group", "leaf"), None, None),
            P("group", "leaf", None),
            P("group", "leaf", None),
            P(("group", "leaf"), None),
            P(("group", "leaf"), None),
        ),
        check_vma=False,
    )
```

```python
import jax
import jax.numpy as jnp
from jax import lax
from jax.sharding import PartitionSpec as P


def to_middle(stacked, onehot, block_count, block_size):
    rows_total, width_total = stacked.shape
    moved = jnp.einsum(
        "lbk,bj->ljk",
        stacked.reshape(rows_total, block_count, block_size),
        onehot,
        preferred_element_type=jnp.float32,
    )
    return moved.astype(jnp.bfloat16).reshape(rows_total, width_total)


def left_product(first_operand, second_operand):
    return lax.dot_general(
        first_operand, second_operand, (((0,), (0,)), ((), ())), preferred_element_type=jnp.float32
    )


def body(
    leaf_mass,
    leaf_damp,
    mass_coupling,
    damp_coupling,
    leaf_modes,
    interface_blocks,
    mid_modes,
    mid_constraint,
):
    leaf_order = leaf_mass.shape[1]
    block_count = interface_blocks.shape[1]
    sep_width = leaf_modes.shape[2]
    block_size = sep_width // block_count
    mode_count = mid_modes.shape[2]
    root_width = mid_constraint.shape[2]
    basis_width = mode_count + root_width
    leaf_count = lax.axis_size("leaf")
    group_count = lax.axis_size("group")
    onehot = (
        interface_blocks[0][:, None] == jnp.arange(block_count, dtype=jnp.int32)[None, :]
    ).astype(jnp.bfloat16)
    placed = to_middle(
        jnp.concatenate([leaf_modes[0], mass_coupling[0], damp_coupling[0]], axis=0),
        onehot,
        block_count,
        block_size,
    )
    constraint = placed[:leaf_order]
    sides = placed[leaf_order:].astype(jnp.float32)
    product = jnp.dot(
        jnp.concatenate([leaf_mass[0], leaf_damp[0]], axis=0),
        constraint,
        preferred_element_type=jnp.float32,
    )
    half_work = (0.5 * product + sides).astype(jnp.bfloat16)
    full_work = (product + sides).astype(jnp.bfloat16)
    basis_rows = jnp.concatenate([mid_modes[0], mid_constraint[0]], axis=1)
    mode_basis = lax.all_gather(basis_rows, "leaf", axis=0, tiled=True)
    left_sum = jnp.dot(constraint, mode_basis, preferred_element_type=jnp.float32)
    right_sum = jnp.dot(half_work, mode_basis, preferred_element_type=jnp.float32)
    coupling = jnp.dot(full_work, mode_basis[:, :mode_count], preferred_element_type=jnp.float32)
    left_part = left_sum.astype(jnp.bfloat16)
    right_part = right_sum.astype(jnp.bfloat16)
    right_mass = right_part[:leaf_order]
    right_damp = right_part[leaf_order:]

    def projected_rows(first_row, amount, first_col):
        left_rows = lax.dynamic_slice_in_dim(left_part, first_row, amount, 1)
        right_rows = lax.dynamic_slice_in_dim(right_part, first_row, amount, 1)
        left_cols = left_part[:, first_col:]
        mass_term = left_product(left_rows, right_mass[:, first_col:]) + left_product(
            right_rows[:leaf_order], left_cols
        )
        damp_term = left_product(left_rows, right_damp[:, first_col:]) + left_product(
            right_rows[leaf_order:], left_cols
        )
        return jnp.concatenate([mass_term, damp_term], axis=1)

    modal_rows, left_ready, mass_ready, damp_ready = lax.optimization_barrier(
        (projected_rows(jnp.int32(0), mode_count, 0), left_part, right_mass, right_damp)
    )
    modal_part = lax.psum_scatter(modal_rows, "leaf", scatter_dimension=0, tiled=True)
    device_count = group_count * leaf_count
    core_odd = lax.axis_index("group") % 2 == 1
    left_root = left_ready[:, mode_count:]
    mass_root = mass_ready[:, mode_count:]
    damp_root = damp_ready[:, mode_count:]
    own_right = jnp.where(core_odd, damp_root, mass_root)
    other_right = jnp.where(core_odd, mass_root, damp_root)
    partner = lax.ppermute(
        jnp.concatenate([left_root, other_right], axis=0),
        "group",
        [(index, index ^ 1) for index in range(group_count)],
    )
    left_pair = jnp.concatenate([left_root, partner[:leaf_order]], axis=0)
    right_pair = jnp.concatenate([own_right, partner[leaf_order:]], axis=0)
    root_rows = left_product(left_pair, right_pair) + left_product(right_pair, left_pair)
    root_recv = lax.all_to_all(
        root_rows.reshape(device_count, root_width // device_count, root_width).astype(jnp.bfloat16),
        ("group", "leaf"),
        0,
        0,
        tiled=True,
    )
    root_part = jnp.sum(
        root_recv.reshape(
            group_count // 2, 2, leaf_count, root_width // device_count, root_width
        ).astype(jnp.float32),
        axis=(0, 2),
    )
    return (
        coupling[:leaf_order][None],
        coupling[leaf_order:][None],
        modal_part[:, :basis_width][None],
        modal_part[:, basis_width:][None],
        root_part[0],
        root_part[1],
    )


def solution(mesh):
    return jax.shard_map(
        body,
        mesh=mesh,
        in_specs=(
            P(("group", "leaf"), None, None),
            P(("group", "leaf"), None, None),
            P(("group", "leaf"), None, None),
            P(("group", "leaf"), None, None),
            P(("group", "leaf"), None, None),
            P(("group", "leaf"), None),
            P("group", "leaf", None),
            P("group", "leaf", None),
        ),
        out_specs=(
            P(("group", "leaf"), None, None),
            P(("group", "leaf"), None, None),
            P("group", "leaf", None),
            P("group", "leaf", None),
            P(("group", "leaf"), None),
            P(("group", "leaf"), None),
        ),
        check_vma=False,
    )
```
